256 devices in a mesh: tile: 64 (over y, z_lo, x, core), date: 4 (over z_hi).
Axes of the slice: x: 4, y: 4, z: 8 (z_hi: 4, z_lo: 2; z = z_hi * 2 + z_lo), core: 2. Of those that a mesh axis runs over, the one named last changes fastest.
Arguments:
- stacks: bfloat16 [64, 16, 64, 64, 128], P('tile', 'date'), may hold values from -6 to 6
- valid: int32 [64, 16], P('tile', 'date'), may hold values 0 or 1
- labels: int32 [64, 64], P('tile'), may hold values from 0 to 19
- w_spatial: bfloat16 [3, 3, 128, 128], replicated, may hold values from -0.1875 to 0.1875
- w_temporal: bfloat16 [5, 128, 128], replicated, may hold values from -0.25 to 0.25
- w_class: bfloat16 [128, 20], replicated, may hold values from -0.5 to 0.5
Outputs:
- dir_spatial: float32 [3, 3, 128, 128], replicated
- dir_temporal: float32 [5, 128, 128], replicated
- dir_class: float32 [128, 20], replicated
The draws below stay inside these ranges and needn't reach their ends.
All inputs are finite; a program needn't handle non-finite values. No bound on the sum of `valid` on one device may be relied on, other than what follows from the above.
Results may differ from the reference program's by a relative error of at most 0.0012.
Values may be sent and summed in bfloat16 or wider, within the bound.
No kernel may reach another device: no remote copies, remote signals or barrier semaphores. Data moves between devices by JAX's collectives and lax.ppermute only.
A program may use at most 192 MiB of HBM per device.

```python
import math
import jax
import jax.numpy as jnp
import numpy as np
from jax import lax

C = 128
CLASSES = 20
WIN = 64
POOL = 8
TAPS = 5
TILES = 64
DATES = 16
BLOCKS = 64


def set_ends(array, rng, smallest, largest):
    shape = array.shape
    index_at = [jax.random.randint(jax.random.fold_in(rng, axis), (), 0, shape[axis]) for axis in range(len(shape))]
    array = array.at[tuple(index_at)].set(smallest)
    longest = shape.index(max(shape))
    index_at[longest] = (index_at[longest] + 1) % shape[longest]
    return array.at[tuple(index_at)].set(largest)


def levels(stream_key, shape, split, least, top_value):
    factor_of, own = 1.0, jax.random.fold_in(stream_key, 6)
    for axis_at, blocks in split:
        steps = jnp.exp(jax.random.uniform(jax.random.fold_in(own, axis_at), (blocks,), jnp.float32, least / len(split), top_value / len(split)))
        factor_of = factor_of * jnp.repeat(steps, shape[axis_at] // blocks).reshape([-1 if axis == axis_at else 1 for axis in range(len(shape))])
    return factor_of


def cumulative_ranks(count, slope):
    weights = [(1 << 20) // math.isqrt(rank ** slope) + 1 for rank in range(1, count + 1)]
    scale = 1 + sum(weights) // (1 << 30)
    return np.cumsum(np.array([max(1, weight // scale) for weight in weights]))


def skewed_ids(own_key, shape, count, slope):
    listing = cumulative_ranks(count, slope)
    pick = jax.random.randint(jax.random.fold_in(own_key, 1), shape, 0, int(listing[count - 1]))
    standing = jnp.searchsorted(jnp.asarray(listing, jnp.int32), pick, side="right")
    return jax.random.permutation(jax.random.fold_in(own_key, 2), count)[standing].astype(jnp.int32)


def gaussian(rng, shape, width, bound, pieces=(), held_as=jnp.bfloat16):
    drawn = width * jax.random.normal(rng, shape, jnp.float32)
    if pieces:
        drawn = drawn * levels(rng, shape, pieces, -0.22, 0.18)
    return jnp.clip(drawn, -bound, bound).astype(held_as)


def setup_inputs(seed: int = 0) -> dict:
    arg_keys = jax.random.split(jax.random.key(seed), 7)
    return {
        "stacks": gaussian(arg_keys[0], (TILES, DATES, WIN, WIN, C), 1.0, 6.0, ((0, 64), (1, 4))),
        "valid": set_ends((jax.random.randint(arg_keys[1], (TILES, DATES), 0, 4) < 3).astype(jnp.int32), jax.random.fold_in(arg_keys[1], 1), 0, 1),
        "labels": set_ends(skewed_ids(arg_keys[2], (TILES, BLOCKS), CLASSES, 2), jax.random.fold_in(arg_keys[2], 3), 0, CLASSES - 1).astype(jnp.int32),
        "w_spatial": gaussian(arg_keys[3], (3, 3, C, C), (9 * C) ** -0.5, 0.1875),
        "w_temporal": gaussian(arg_keys[4], (TAPS, C, C), (TAPS * C) ** -0.5, 0.25),
        "w_class": gaussian(arg_keys[5], (C, CLASSES), C ** -0.5, 0.5),
    }


EPSILON = 1e-06

def silu_pair(value):
    sigma = jax.nn.sigmoid(value)
    return (value * sigma, sigma * (1.0 + value * (1.0 - sigma)))

def spatial_windows(frames):
    extent = frames.shape[1]
    padded = jnp.pad(frames, ((0, 0), (1, 1), (1, 1), (0, 0)))
    return [padded[:, row_shift:row_shift + extent, col_shift:col_shift + extent, :] for row_shift in range(3) for col_shift in range(3)]

def spatial_conv(frames, w_spatial):
    windows = spatial_windows(frames)
    channels = frames.shape[-1]
    running = jnp.zeros(frames.shape, jnp.float32)
    for offset in range(9):
        product = jnp.dot(windows[offset].reshape(-1, channels), w_spatial[offset // 3, offset % 3], preferred_element_type=jnp.float32)
        running = running + product.reshape(frames.shape)
    return running

def block_mean(activation):
    frames, extent, _, channels = activation.shape
    per_side = extent // POOL
    shaped = activation.reshape(frames, per_side, POOL, per_side, POOL, channels)
    return lax.optimization_barrier(jnp.mean(shaped, axis=(2, 4))).reshape(frames, per_side * per_side, channels)

def block_spread(block_values, extent):
    frames, _, channels = block_values.shape
    per_side = extent // POOL
    spread = jnp.broadcast_to(block_values.reshape(frames, per_side, 1, per_side, 1, channels), (frames, per_side, POOL, per_side, POOL, channels))
    return spread.reshape(frames, extent, extent, channels)

def normalize(gradient):
    return gradient / jnp.sqrt(jnp.mean(gradient * gradient) + EPSILON)

def reference(stacks, valid, labels, w_spatial, w_temporal, w_class):
    valid_float = valid.astype(jnp.float32)
    channels = stacks.shape[-1]

    def pool_tile(element):
        frames, flag_rows = element
        activation, _ = silu_pair(spatial_conv(frames, w_spatial))
        return (block_mean(activation) * flag_rows[:, None, None]).astype(jnp.bfloat16)
    pooled = lax.map(pool_tile, (stacks, valid_float))
    extended = jnp.pad(pooled, ((0, 0), (2, 2), (0, 0), (0, 0)))
    response_in = jnp.zeros(pooled.shape, jnp.float32)
    for offset in range(TAPS):
        product = jnp.dot(extended[:, offset:offset + DATES].reshape(-1, channels), w_temporal[offset], preferred_element_type=jnp.float32)
        response_in = response_in + product.reshape(pooled.shape)
    response, response_slope = silu_pair(response_in)
    summary = lax.optimization_barrier(jnp.sum(response, axis=1)) / DATES
    summary_b = summary.astype(jnp.bfloat16).reshape(-1, channels)
    logits = jnp.dot(summary_b, w_class, preferred_element_type=jnp.float32)
    exponent = jnp.exp(logits)
    probability = exponent / lax.optimization_barrier(jnp.sum(exponent, axis=-1, keepdims=True))
    onehot = (labels.reshape(-1, 1) == jnp.arange(CLASSES, dtype=jnp.int32)[None, :]).astype(jnp.float32)
    class_slope = (probability - onehot).astype(jnp.bfloat16)
    grad_class = jnp.dot(summary_b.T, class_slope, preferred_element_type=jnp.float32)
    back_sum = jnp.dot(class_slope, w_class.T, preferred_element_type=jnp.float32).reshape(summary.shape)
    back_q = ((back_sum / DATES)[:, None] * response_slope).astype(jnp.bfloat16)
    flat_q = back_q.reshape(-1, channels)
    grad_temporal = jnp.stack([jnp.dot(extended[:, offset:offset + DATES].reshape(-1, channels).T, flat_q, preferred_element_type=jnp.float32) for offset in range(TAPS)])
    back_ext = jnp.pad(back_q, ((0, 0), (2, 2), (0, 0), (0, 0)))
    back_pool = jnp.zeros(pooled.shape, jnp.float32)
    for offset in range(TAPS):
        product = jnp.dot(back_ext[:, 4 - offset:4 - offset + DATES].reshape(-1, channels), w_temporal[offset].T, preferred_element_type=jnp.float32)
        back_pool = back_pool + product.reshape(pooled.shape)
    back_block = back_pool * valid_float[:, :, None, None] / (POOL * POOL)

    def spatial_grad(running, element):
        frames, block_terms = element
        _, h_slope = silu_pair(spatial_conv(frames, w_spatial))
        back_h = (block_spread(block_terms, frames.shape[1]) * h_slope).astype(jnp.bfloat16)
        flat_h = back_h.reshape(-1, channels)
        windows = spatial_windows(frames)
        partial_grad = jnp.stack([jnp.dot(window.reshape(-1, channels).T, flat_h, preferred_element_type=jnp.float32) for window in windows])
        return (running + partial_grad.reshape(3, 3, channels, channels), None)
    grad_spatial, _ = lax.scan(spatial_grad, jnp.zeros((3, 3, channels, channels), jnp.float32), (stacks, back_block))
    return (normalize(grad_spatial), normalize(grad_temporal), normalize(grad_class))
```

```python
import jax
import jax.numpy as jnp
from jax import lax
from jax.sharding import PartitionSpec as P

POOL = 8


EPSILON = 1e-06


def padded_2(block, sides, width):
    for axis, dim in sides:
        count = lax.axis_size(axis)
        forward = [(i, i + 1) for i in range(count - 1)]
        backward = [(target, source) for source, target in forward]
        low = lax.ppermute(
            lax.slice_in_dim(block, block.shape[dim] - width, None, axis=dim), axis, forward
        )
        high = lax.ppermute(lax.slice_in_dim(block, 0, width, axis=dim), axis, backward)
        block = jnp.concatenate([low, block, high], axis=dim)
    return block


def silu_pair(value):
    sigma = jax.nn.sigmoid(value)
    return (value * sigma, sigma * (1.0 + value * (1.0 - sigma)))


def spatial_windows(frames):
    extent = frames.shape[1]
    padded = jnp.pad(frames, ((0, 0), (1, 1), (1, 1), (0, 0)))
    return [
        padded[:, row_shift : row_shift + extent, col_shift : col_shift + extent, :]
        for row_shift in range(3)
        for col_shift in range(3)
    ]


def spatial_forward(frames, w_spatial):
    windows = spatial_windows(frames)
    running = jnp.zeros(frames.shape, jnp.float32)
    for offset in range(9):
        running = running + jnp.einsum(
            "fyxc,ce->fyxe",
            windows[offset],
            w_spatial[offset // 3, offset % 3],
            preferred_element_type=jnp.float32,
        )
    return running


def block_mean(activation):
    frames, extent, _, channels = activation.shape
    per_side = extent // POOL
    shaped = activation.reshape(frames, per_side, POOL, per_side, POOL, channels)
    return jnp.mean(shaped, axis=(2, 4)).reshape(frames, per_side * per_side, channels)


def block_spread(block_values, extent):
    frames, _, channels = block_values.shape
    per_side = extent // POOL
    spread = jnp.broadcast_to(
        block_values.reshape(frames, per_side, 1, per_side, 1, channels),
        (frames, per_side, POOL, per_side, POOL, channels),
    )
    return spread.reshape(frames, extent, extent, channels)


def temporal_forward(extended, w_temporal, count):
    running = jnp.zeros(
        (extended.shape[0], count, extended.shape[2], extended.shape[3]), jnp.float32
    )
    for offset in range(w_temporal.shape[0]):
        running = running + jnp.einsum(
            "tdbc,ce->tdbe",
            extended[:, offset : offset + count],
            w_temporal[offset],
            preferred_element_type=jnp.float32,
        )
    return running


def classify(summary_b, label_rows, w_class):
    logits = jnp.einsum("tbc,ck->tbk", summary_b, w_class, preferred_element_type=jnp.float32)
    exponent = jnp.exp(logits)
    probability = exponent / jnp.sum(exponent, axis=-1, keepdims=True)
    onehot = (
        label_rows[:, :, None] == jnp.arange(w_class.shape[1], dtype=jnp.int32)[None, None, :]
    ).astype(jnp.float32)
    class_slope = (probability - onehot).astype(jnp.bfloat16)
    back_sum = jnp.einsum("tbk,ck->tbc", class_slope, w_class, preferred_element_type=jnp.float32)
    return (class_slope, back_sum)


def normalize(gradient):
    return gradient / jnp.sqrt(jnp.mean(gradient * gradient) + EPSILON)


def exchange_steps():
    tile_bits = lax.axis_size("tile").bit_length() - 1
    date_bits = lax.axis_size("date").bit_length() - 1
    assert 1 << tile_bits == lax.axis_size("tile") and 1 << date_bits == lax.axis_size("date")
    tile_order = list(range(tile_bits))
    if tile_bits == 6:
        tile_order = [0, 3, 1, 2, 4, 5]
    steps = [("tile", 1 << tile_order[0])]
    steps += [("date", 1 << bit) for bit in range(date_bits)]
    steps += [("tile", 1 << bit) for bit in tile_order[1:]]
    return steps


def all_sum(parts):
    lanes = 128
    flat = jnp.concatenate([part.reshape(-1) for part in parts])
    steps = exchange_steps()
    unit = 8 << len(steps)
    rows = -(-flat.shape[0] // (lanes * unit)) * unit
    buf = jnp.pad(flat, (0, rows * lanes - flat.shape[0])).reshape(rows, lanes)
    for axis, mask in steps:
        count = lax.axis_size(axis)
        pairs = [(i, i ^ mask) for i in range(count)]
        upper = (lax.axis_index(axis) // mask) % 2
        half = buf.shape[0] // 2
        keep = lax.dynamic_slice_in_dim(buf, upper * half, half)
        send = lax.dynamic_slice_in_dim(buf, (1 - upper) * half, half)
        buf = keep + lax.ppermute(send, axis, pairs)
    for axis, mask in reversed(steps):
        count = lax.axis_size(axis)
        pairs = [(i, i ^ mask) for i in range(count)]
        upper = (lax.axis_index(axis) // mask) % 2
        other = lax.ppermute(buf, axis, pairs)
        buf = jnp.where(
            upper == 1, jnp.concatenate([other, buf]), jnp.concatenate([buf, other])
        )
    flat = buf.reshape(-1)
    out, start = [], 0
    for part in parts:
        out.append(flat[start : start + part.size].reshape(part.shape))
        start += part.size
    return out


def shards(stacks, valid, labels, w_spatial, w_temporal, w_class):
    tile_dev, date_dev, extent, _, channels = stacks.shape
    frames = stacks.reshape(tile_dev * date_dev, extent, extent, channels)
    pre_act = spatial_forward(frames, w_spatial)
    activation, h_slope = silu_pair(pre_act)
    valid_float = valid.astype(jnp.float32)
    pooled = block_mean(activation).reshape(tile_dev, date_dev, -1, channels)
    blocks = pooled.shape[2]
    pooled_b = (pooled * valid_float[:, :, None, None]).astype(jnp.bfloat16)
    date_count = lax.axis_size("date")
    date_total = date_count * date_dev
    share = blocks // date_count
    share_start = lax.axis_index("date") * share
    extended = padded_2(pooled_b, (("date", 1),), 2)
    response, response_slope = silu_pair(temporal_forward(extended, w_temporal, date_dev))
    partial_sum = jnp.sum(response, axis=1)
    summary = lax.psum(partial_sum, "date") / date_total
    summary_b = summary.astype(jnp.bfloat16)
    class_slope, back_sum = classify(summary_b, labels, w_class)
    own_summary = lax.dynamic_slice_in_dim(summary_b, share_start, share, 1)
    own_slope = lax.dynamic_slice_in_dim(class_slope, share_start, share, 1)
    grad_class = jnp.einsum(
        "tbc,tbk->ck", own_summary, own_slope, preferred_element_type=jnp.float32
    )
    scaled = back_sum / date_total
    back_q = (scaled[:, None] * response_slope).astype(jnp.bfloat16)
    back_ext = padded_2(back_q, (("date", 1),), 2)
    taps = w_temporal.shape[0]
    grad_temporal = jnp.stack(
        [
            jnp.einsum(
                "tdbc,tdbe->ce",
                extended[:, offset : offset + date_dev],
                back_q,
                preferred_element_type=jnp.float32,
            )
            for offset in range(taps)
        ]
    )
    back_pool = jnp.zeros(pooled.shape, jnp.float32)
    for offset in range(taps):
        back_pool = back_pool + jnp.einsum(
            "tdbe,ce->tdbc",
            back_ext[:, 4 - offset : 4 - offset + date_dev],
            w_temporal[offset],
            preferred_element_type=jnp.float32,
        )
    back_block = (back_pool * valid_float[:, :, None, None] / (POOL * POOL)).reshape(
        tile_dev * date_dev, blocks, channels
    )
    back_h = (block_spread(back_block, extent) * h_slope).astype(jnp.bfloat16)
    windows = spatial_windows(frames)
    grad_spatial = jnp.stack(
        [
            jnp.einsum("fyxc,fyxe->ce", window, back_h, preferred_element_type=jnp.float32)
            for window in windows
        ]
    ).reshape(3, 3, channels, channels)
    total_spatial, total_temporal, total_class = all_sum(
        (grad_spatial, grad_temporal, grad_class)
    )
    return (normalize(total_spatial), normalize(total_temporal), normalize(total_class))


def solution(mesh):
    in_specs = (
        P("tile", "date", None, None, None),
        P("tile", "date"),
        P("tile", None),
        P(),
        P(),
        P(),
    )
    out_specs = (P(), P(), P())
    return jax.shard_map(shards, mesh=mesh, in_specs=in_specs, out_specs=out_specs, check_vma=False)
```

```python
import jax
import jax.numpy as jnp
from jax import lax
from jax.sharding import PartitionSpec as P

POOL = 8


EPSILON = 1e-06


def padded_2(block, sides, width):
    for axis, dim in sides:
        count = lax.axis_size(axis)
        forward = [(i, i + 1) for i in range(count - 1)]
        backward = [(target, source) for source, target in forward]
        low = lax.ppermute(
            lax.slice_in_dim(block, block.shape[dim] - width, None, axis=dim), axis, forward
        )
        high = lax.ppermute(lax.slice_in_dim(block, 0, width, axis=dim), axis, backward)
        block = jnp.concatenate([low, block, high], axis=dim)
    return block


def silu_pair(value):
    sigma = jax.nn.sigmoid(value)
    return (value * sigma, sigma * (1.0 + value * (1.0 - sigma)))


def spatial_windows(frames):
    extent = frames.shape[1]
    padded = jnp.pad(frames, ((0, 0), (1, 1), (1, 1), (0, 0)))
    return [
        padded[:, row_shift : row_shift + extent, col_shift : col_shift + extent, :]
        for row_shift in range(3)
        for col_shift in range(3)
    ]


def spatial_forward(frames, w_spatial):
    return lax.conv_general_dilated(
        frames,
        w_spatial,
        (1, 1),
        ((1, 1), (1, 1)),
        dimension_numbers=("NHWC", "HWIO", "NHWC"),
        preferred_element_type=jnp.float32,
    )


def date_sum(value):
    count = lax.axis_size("date")
    mask = 1
    while mask < count:
        value = value + lax.ppermute(value, "date", [(i, i ^ mask) for i in range(count)])
        mask *= 2
    return value


def block_mean(activation):
    frames, extent, _, channels = activation.shape
    per_side = extent // POOL
    shaped = activation.reshape(frames, per_side, POOL, per_side, POOL, channels)
    return jnp.mean(shaped, axis=(2, 4)).reshape(frames, per_side * per_side, channels)


def block_spread(block_values, extent):
    frames, _, channels = block_values.shape
    per_side = extent // POOL
    spread = jnp.broadcast_to(
        block_values.reshape(frames, per_side, 1, per_side, 1, channels),
        (frames, per_side, POOL, per_side, POOL, channels),
    )
    return spread.reshape(frames, extent, extent, channels)


def temporal_forward(extended, w_temporal, count):
    running = jnp.zeros(
        (extended.shape[0], count, extended.shape[2], extended.shape[3]), jnp.float32
    )
    for offset in range(w_temporal.shape[0]):
        running = running + jnp.einsum(
            "tdbc,ce->tdbe",
            extended[:, offset : offset + count],
            w_temporal[offset],
            preferred_element_type=jnp.float32,
        )
    return running


def classify(summary_b, label_rows, w_class):
    logits = jnp.einsum("tbc,ck->tbk", summary_b, w_class, preferred_element_type=jnp.float32)
    exponent = jnp.exp(logits)
    probability = exponent / jnp.sum(exponent, axis=-1, keepdims=True)
    onehot = (
        label_rows[:, :, None] == jnp.arange(w_class.shape[1], dtype=jnp.int32)[None, None, :]
    ).astype(jnp.float32)
    class_slope = (probability - onehot).astype(jnp.bfloat16)
    back_sum = jnp.einsum("tbk,ck->tbc", class_slope, w_class, preferred_element_type=jnp.float32)
    return (class_slope, back_sum)


def normalize(gradient):
    return gradient / jnp.sqrt(jnp.mean(gradient * gradient) + EPSILON)


def exchange_steps():
    tile_bits = lax.axis_size("tile").bit_length() - 1
    date_bits = lax.axis_size("date").bit_length() - 1
    assert 1 << tile_bits == lax.axis_size("tile") and 1 << date_bits == lax.axis_size("date")
    tile_order = list(range(tile_bits))
    if tile_bits == 6:
        tile_order = [0, 3, 1, 2, 4, 5]
    steps = [("tile", 1 << tile_order[0])]
    steps += [("date", 1 << bit) for bit in range(date_bits)]
    steps += [("tile", 1 << bit) for bit in tile_order[1:]]
    return steps


def all_sum(parts):
    lanes = 128
    flat = jnp.concatenate([part.reshape(-1) for part in parts])
    steps = exchange_steps()
    unit = 8 << len(steps)
    rows = -(-flat.shape[0] // (lanes * unit)) * unit
    buf = jnp.pad(flat, (0, rows * lanes - flat.shape[0])).reshape(rows, lanes)
    for axis, mask in steps:
        count = lax.axis_size(axis)
        pairs = [(i, i ^ mask) for i in range(count)]
        upper = (lax.axis_index(axis) // mask) % 2
        half = buf.shape[0] // 2
        keep = lax.dynamic_slice_in_dim(buf, upper * half, half)
        send = lax.dynamic_slice_in_dim(buf, (1 - upper) * half, half)
        buf = keep + lax.ppermute(send, axis, pairs)
    for axis, mask in reversed(steps):
        count = lax.axis_size(axis)
        pairs = [(i, i ^ mask) for i in range(count)]
        upper = (lax.axis_index(axis) // mask) % 2
        other = lax.ppermute(buf, axis, pairs)
        buf = jnp.where(
            upper == 1, jnp.concatenate([other, buf]), jnp.concatenate([buf, other])
        )
    flat = buf.reshape(-1)
    out, start = [], 0
    for part in parts:
        out.append(flat[start : start + part.size].reshape(part.shape))
        start += part.size
    return out


def shards(stacks, valid, labels, w_spatial, w_temporal, w_class):
    tile_dev, date_dev, extent, _, channels = stacks.shape
    frames = stacks.reshape(tile_dev * date_dev, extent, extent, channels)
    pre_act = spatial_forward(frames, w_spatial)
    activation, h_slope = silu_pair(pre_act)
    valid_float = valid.astype(jnp.float32)
    pooled = block_mean(activation).reshape(tile_dev, date_dev, -1, channels)
    blocks = pooled.shape[2]
    pooled_b = (pooled * valid_float[:, :, None, None]).astype(jnp.bfloat16)
    date_count = lax.axis_size("date")
    date_total = date_count * date_dev
    share = blocks // date_count
    share_start = lax.axis_index("date") * share
    extended = padded_2(pooled_b, (("date", 1),), 2)
    response, response_slope = silu_pair(temporal_forward(extended, w_temporal, date_dev))
    partial_sum = jnp.sum(response, axis=1)
    summary = date_sum(partial_sum) / date_total
    summary_b = summary.astype(jnp.bfloat16)
    class_slope, back_sum = classify(summary_b, labels, w_class)
    own_summary = lax.dynamic_slice_in_dim(summary_b, share_start, share, 1)
    own_slope = lax.dynamic_slice_in_dim(class_slope, share_start, share, 1)
    grad_class = jnp.einsum(
        "tbc,tbk->ck", own_summary, own_slope, preferred_element_type=jnp.float32
    )
    scaled = back_sum / date_total
    back_q = (scaled[:, None] * response_slope).astype(jnp.bfloat16)
    back_ext = padded_2(back_q, (("date", 1),), 2)
    taps = w_temporal.shape[0]
    grad_temporal = jnp.stack(
        [
            jnp.einsum(
                "tdbc,tdbe->ce",
                extended[:, offset : offset + date_dev],
                back_q,
                preferred_element_type=jnp.float32,
            )
            for offset in range(taps)
        ]
    )
    back_pool = jnp.zeros(pooled.shape, jnp.float32)
    for offset in range(taps):
        back_pool = back_pool + jnp.einsum(
            "tdbe,ce->tdbc",
            back_ext[:, 4 - offset : 4 - offset + date_dev],
            w_temporal[offset],
            preferred_element_type=jnp.float32,
        )
    back_block = (back_pool * valid_float[:, :, None, None] / (POOL * POOL)).reshape(
        tile_dev * date_dev, blocks, channels
    )
    back_h = (block_spread(back_block, extent) * h_slope).astype(jnp.bfloat16)
    windows = spatial_windows(frames)
    grad_spatial = jnp.stack(
        [
            jnp.einsum("fyxc,fyxe->ce", window, back_h, preferred_element_type=jnp.float32)
            for window in windows
        ]
    ).reshape(3, 3, channels, channels)
    total_spatial, total_temporal, total_class = all_sum(
        (grad_spatial, grad_temporal, grad_class)
    )
    return (normalize(total_spatial), normalize(total_temporal), normalize(total_class))


def solution(mesh):
    in_specs = (
        P("tile", "date", None, None, None),
        P("tile", "date"),
        P("tile", None),
        P(),
        P(),
        P(),
    )
    out_specs = (P(), P(), P())
    return jax.shard_map(shards, mesh=mesh, in_specs=in_specs, out_specs=out_specs, check_vma=False)
```

```python
import jax
import jax.numpy as jnp
from jax import lax
from jax.sharding import PartitionSpec as P

POOL = 8


EPSILON = 1e-06


def padded_2(block, sides, width):
    for axis, dim in sides:
        count = lax.axis_size(axis)
        forward = [(i, i + 1) for i in range(count - 1)]
        backward = [(target, source) for source, target in forward]
        low = lax.ppermute(
            lax.slice_in_dim(block, block.shape[dim] - width, None, axis=dim), axis, forward
        )
        high = lax.ppermute(lax.slice_in_dim(block, 0, width, axis=dim), axis, backward)
        block = jnp.concatenate([low, block, high], axis=dim)
    return block


def silu_pair(value):
    sigma = jax.nn.sigmoid(value)
    return (value * sigma, sigma * (1.0 + value * (1.0 - sigma)))


def spatial_windows(frames):
    extent = frames.shape[1]
    padded = jnp.pad(frames, ((0, 0), (1, 1), (1, 1), (0, 0)))
    return [
        padded[:, row_shift : row_shift + extent, col_shift : col_shift + extent, :]
        for row_shift in range(3)
        for col_shift in range(3)
    ]


def spatial_forward(frames, w_spatial):
    return lax.conv_general_dilated(
        frames,
        w_spatial,
        (1, 1),
        ((1, 1), (1, 1)),
        dimension_numbers=("NHWC", "HWIO", "NHWC"),
        preferred_element_type=jnp.float32,
    )


def date_sum(value):
    count = lax.axis_size("date")
    mask = 1
    while mask < count:
        value = value + lax.ppermute(value, "date", [(i, i ^ mask) for i in range(count)])
        mask *= 2
    return value


def block_mean(activation):
    frames, extent, _, channels = activation.shape
    per_side = extent // POOL
    shaped = activation.reshape(frames, per_side, POOL, per_side, POOL, channels)
    return jnp.mean(shaped, axis=(2, 4)).reshape(frames, per_side * per_side, channels)


def block_spread(block_values, extent):
    frames, _, channels = block_values.shape
    per_side = extent // POOL
    spread = jnp.broadcast_to(
        block_values.reshape(frames, per_side, 1, per_side, 1, channels),
        (frames, per_side, POOL, per_side, POOL, channels),
    )
    return spread.reshape(frames, extent, extent, channels)


def temporal_forward(extended, w_temporal, count):
    running = jnp.zeros(
        (extended.shape[0], count, extended.shape[2], extended.shape[3]), jnp.float32
    )
    for offset in range(w_temporal.shape[0]):
        running = running + jnp.einsum(
            "tdbc,ce->tdbe",
            extended[:, offset : offset + count],
            w_temporal[offset],
            preferred_element_type=jnp.float32,
        )
    return running


def classify(summary_b, label_rows, w_class):
    logits = jnp.einsum("tbc,ck->tbk", summary_b, w_class, preferred_element_type=jnp.float32)
    exponent = jnp.exp(logits)
    probability = exponent / jnp.sum(exponent, axis=-1, keepdims=True)
    onehot = (
        label_rows[:, :, None] == jnp.arange(w_class.shape[1], dtype=jnp.int32)[None, None, :]
    ).astype(jnp.float32)
    class_slope = (probability - onehot).astype(jnp.bfloat16)
    back_sum = jnp.einsum("tbk,ck->tbc", class_slope, w_class, preferred_element_type=jnp.float32)
    return (class_slope, back_sum)


def normalize(gradient):
    return gradient / jnp.sqrt(jnp.mean(gradient * gradient) + EPSILON)


def exchange_groups():
    tile_bits = lax.axis_size("tile").bit_length() - 1
    date_bits = lax.axis_size("date").bit_length() - 1
    assert 1 << tile_bits == lax.axis_size("tile") and 1 << date_bits == lax.axis_size("date")
    if tile_bits == 6 and date_bits == 2:
        return [[2], [5, 0, 1], [3, 4], [6, 7]]
    return [[bit] for bit in range(tile_bits + date_bits)]


def group_code(index, bits):
    code = 0
    for place, bit in enumerate(bits):
        code = code + ((index >> bit) & 1) * (1 << place)
    return code


def group_mask(code, bits):
    return sum(1 << bit for place, bit in enumerate(bits) if (code >> place) & 1)


def all_sum(parts):
    lanes = 128
    axes = ("tile", "date")
    total = lax.axis_size("tile") * lax.axis_size("date")
    index = lax.axis_index("tile") * lax.axis_size("date") + lax.axis_index("date")
    flat = jnp.concatenate([part.reshape(-1) for part in parts])
    groups = exchange_groups()
    unit = 8 * total
    rows = -(-flat.shape[0] // (lanes * unit)) * unit
    buf = jnp.pad(flat, (0, rows * lanes - flat.shape[0])).reshape(rows, lanes)
    for bits in groups:
        size = buf.shape[0] >> len(bits)
        own = group_code(index, bits)
        acc = lax.dynamic_slice_in_dim(buf, own * size, size)
        for code in range(1, 1 << len(bits)):
            mask = group_mask(code, bits)
            send = lax.dynamic_slice_in_dim(buf, (own ^ code) * size, size)
            acc = acc + lax.ppermute(send, axes, [(i, i ^ mask) for i in range(total)])
        buf = acc
    for bits in reversed(groups):
        size = buf.shape[0]
        own = group_code(index, bits)
        out = jnp.zeros((size << len(bits), lanes), buf.dtype)
        out = lax.dynamic_update_slice_in_dim(out, buf, own * size, 0)
        for code in range(1, 1 << len(bits)):
            mask = group_mask(code, bits)
            got = lax.ppermute(buf, axes, [(i, i ^ mask) for i in range(total)])
            out = lax.dynamic_update_slice_in_dim(out, got, (own ^ code) * size, 0)
        buf = out
    flat = buf.reshape(-1)
    out, start = [], 0
    for part in parts:
        out.append(flat[start : start + part.size].reshape(part.shape))
        start += part.size
    return out


def shards(stacks, valid, labels, w_spatial, w_temporal, w_class):
    tile_dev, date_dev, extent, _, channels = stacks.shape
    frames = stacks.reshape(tile_dev * date_dev, extent, extent, channels)
    pre_act = spatial_forward(frames, w_spatial)
    activation, h_slope = silu_pair(pre_act)
    valid_float = valid.astype(jnp.float32)
    pooled = block_mean(activation).reshape(tile_dev, date_dev, -1, channels)
    blocks = pooled.shape[2]
    pooled_b = (pooled * valid_float[:, :, None, None]).astype(jnp.bfloat16)
    date_count = lax.axis_size("date")
    date_total = date_count * date_dev
    share = blocks // date_count
    share_start = lax.axis_index("date") * share
    extended = padded_2(pooled_b, (("date", 1),), 2)
    response, response_slope = silu_pair(temporal_forward(extended, w_temporal, date_dev))
    partial_sum = jnp.sum(response, axis=1)
    summary = date_sum(partial_sum) / date_total
    summary_b = summary.astype(jnp.bfloat16)
    class_slope, back_sum = classify(summary_b, labels, w_class)
    own_summary = lax.dynamic_slice_in_dim(summary_b, share_start, share, 1)
    own_slope = lax.dynamic_slice_in_dim(class_slope, share_start, share, 1)
    grad_class = jnp.einsum(
        "tbc,tbk->ck", own_summary, own_slope, preferred_element_type=jnp.float32
    )
    scaled = back_sum / date_total
    back_q = (scaled[:, None] * response_slope).astype(jnp.bfloat16)
    back_ext = padded_2(back_q, (("date", 1),), 2)
    taps = w_temporal.shape[0]
    grad_temporal = jnp.stack(
        [
            jnp.einsum(
                "tdbc,tdbe->ce",
                extended[:, offset : offset + date_dev],
                back_q,
                preferred_element_type=jnp.float32,
            )
            for offset in range(taps)
        ]
    )
    back_pool = jnp.zeros(pooled.shape, jnp.float32)
    for offset in range(taps):
        back_pool = back_pool + jnp.einsum(
            "tdbe,ce->tdbc",
            back_ext[:, 4 - offset : 4 - offset + date_dev],
            w_temporal[offset],
            preferred_element_type=jnp.float32,
        )
    back_block = (back_pool * valid_float[:, :, None, None] / (POOL * POOL)).reshape(
        tile_dev * date_dev, blocks, channels
    )
    back_h = (block_spread(back_block, extent) * h_slope).astype(jnp.bfloat16)
    windows = spatial_windows(frames)
    grad_spatial = jnp.stack(
        [
            jnp.einsum("fyxc,fyxe->ce", window, back_h, preferred_element_type=jnp.float32)
            for window in windows
        ]
    ).reshape(3, 3, channels, channels)
    total_spatial, total_temporal, total_class = all_sum(
        (grad_spatial, grad_temporal, grad_class)
    )
    return (normalize(total_spatial), normalize(total_temporal), normalize(total_class))


def solution(mesh):
    in_specs = (
        P("tile", "date", None, None, None),
        P("tile", "date"),
        P("tile", None),
        P(),
        P(),
        P(),
    )
    out_specs = (P(), P(), P())
    return jax.shard_map(shards, mesh=mesh, in_specs=in_specs, out_specs=out_specs, check_vma=False)
```

```python
import jax
import jax.numpy as jnp
from jax import lax
from jax.sharding import PartitionSpec as P

POOL = 8


EPSILON = 1e-06


def padded_2(block, sides, width):
    for axis, dim in sides:
        count = lax.axis_size(axis)
        forward = [(i, i + 1) for i in range(count - 1)]
        backward = [(target, source) for source, target in forward]
        low = lax.ppermute(
            lax.slice_in_dim(block, block.shape[dim] - width, None, axis=dim), axis, forward
        )
        high = lax.ppermute(lax.slice_in_dim(block, 0, width, axis=dim), axis, backward)
        block = jnp.concatenate([low, block, high], axis=dim)
    return block


def silu_pair(value):
    sigma = jax.nn.sigmoid(value)
    return (value * sigma, sigma * (1.0 + value * (1.0 - sigma)))


def spatial_windows(frames):
    extent = frames.shape[1]
    padded = jnp.pad(frames, ((0, 0), (1, 1), (1, 1), (0, 0)))
    return [
        padded[:, row_shift : row_shift + extent, col_shift : col_shift + extent, :]
        for row_shift in range(3)
        for col_shift in range(3)
    ]


def spatial_forward(frames, w_spatial):
    return lax.conv_general_dilated(
        frames,
        w_spatial,
        (1, 1),
        ((1, 1), (1, 1)),
        dimension_numbers=("NHWC", "HWIO", "NHWC"),
        preferred_element_type=jnp.float32,
    )


def date_sum(value):
    count = lax.axis_size("date")
    mask = 1
    while mask < count:
        value = value + lax.ppermute(value, "date", [(i, i ^ mask) for i in range(count)])
        mask *= 2
    return value


def block_mean(activation):
    frames, extent, _, channels = activation.shape
    per_side = extent // POOL
    shaped = activation.reshape(frames, per_side, POOL, per_side, POOL, channels)
    return jnp.mean(shaped, axis=(2, 4)).reshape(frames, per_side * per_side, channels)


def block_spread(block_values, extent):
    frames, _, channels = block_values.shape
    per_side = extent // POOL
    spread = jnp.broadcast_to(
        block_values.reshape(frames, per_side, 1, per_side, 1, channels),
        (frames, per_side, POOL, per_side, POOL, channels),
    )
    return spread.reshape(frames, extent, extent, channels)


def temporal_forward(extended, w_temporal, count):
    running = jnp.zeros(
        (extended.shape[0], count, extended.shape[2], extended.shape[3]), jnp.float32
    )
    for offset in range(w_temporal.shape[0]):
        running = running + jnp.einsum(
            "tdbc,ce->tdbe",
            extended[:, offset : offset + count],
            w_temporal[offset],
            preferred_element_type=jnp.float32,
        )
    return running


def classify(summary_b, label_rows, w_class):
    logits = jnp.einsum("tbc,ck->tbk", summary_b, w_class, preferred_element_type=jnp.float32)
    exponent = jnp.exp(logits)
    probability = exponent / jnp.sum(exponent, axis=-1, keepdims=True)
    onehot = (
        label_rows[:, :, None] == jnp.arange(w_class.shape[1], dtype=jnp.int32)[None, None, :]
    ).astype(jnp.float32)
    class_slope = (probability - onehot).astype(jnp.bfloat16)
    back_sum = jnp.einsum("tbk,ck->tbc", class_slope, w_class, preferred_element_type=jnp.float32)
    return (class_slope, back_sum)


def normalize(gradient):
    return gradient / jnp.sqrt(jnp.mean(gradient * gradient) + EPSILON)


def exchange_groups():
    tile_bits = lax.axis_size("tile").bit_length() - 1
    date_bits = lax.axis_size("date").bit_length() - 1
    assert 1 << tile_bits == lax.axis_size("tile") and 1 << date_bits == lax.axis_size("date")
    if tile_bits == 6 and date_bits == 2:
        return [[2], [5, 0, 1], [3, 4], [6, 7]]
    return [[bit] for bit in range(tile_bits + date_bits)]


def group_code(index, bits):
    code = 0
    for place, bit in enumerate(bits):
        code = code + ((index >> bit) & 1) * (1 << place)
    return code


def group_mask(code, bits):
    return sum(1 << bit for place, bit in enumerate(bits) if (code >> place) & 1)


def all_sum(parts):
    lanes = 128
    axes = ("tile", "date")
    total = lax.axis_size("tile") * lax.axis_size("date")
    index = lax.axis_index("tile") * lax.axis_size("date") + lax.axis_index("date")
    flat = jnp.concatenate([part.reshape(-1) for part in parts])
    groups = exchange_groups()
    unit = 8 * total
    rows = -(-flat.shape[0] // (lanes * unit)) * unit
    buf = jnp.pad(flat, (0, rows * lanes - flat.shape[0])).reshape(rows, lanes)
    for bits in groups:
        size = buf.shape[0] >> len(bits)
        own = group_code(index, bits)
        acc = lax.dynamic_slice_in_dim(buf, own * size, size)
        for code in range(1, 1 << len(bits)):
            mask = group_mask(code, bits)
            send = lax.dynamic_slice_in_dim(buf, (own ^ code) * size, size)
            acc = acc + lax.ppermute(send, axes, [(i, i ^ mask) for i in range(total)])
        buf = acc
    for bits in reversed(groups):
        size = buf.shape[0]
        own = group_code(index, bits)
        out = jnp.zeros((size << len(bits), lanes), buf.dtype)
        out = lax.dynamic_update_slice_in_dim(out, buf, own * size, 0)
        for code in range(1, 1 << len(bits)):
            mask = group_mask(code, bits)
            got = lax.ppermute(buf, axes, [(i, i ^ mask) for i in range(total)])
            out = lax.dynamic_update_slice_in_dim(out, got, (own ^ code) * size, 0)
        buf = out
    flat = buf.reshape(-1)
    out, start = [], 0
    for part in parts:
        out.append(flat[start : start + part.size].reshape(part.shape))
        start += part.size
    return out


def date_gather(block):
    count = lax.axis_size("date")
    own = lax.axis_index("date")
    depth = block.shape[1]
    shape = (block.shape[0], depth * count) + block.shape[2:]
    out = lax.dynamic_update_slice_in_dim(jnp.zeros(shape, block.dtype), block, own * depth, 1)
    for mask in range(1, count):
        got = lax.ppermute(block, "date", [(i, i ^ mask) for i in range(count)])
        out = lax.dynamic_update_slice_in_dim(out, got, (own ^ mask) * depth, 1)
    return out


def shards(stacks, valid, labels, w_spatial, w_temporal, w_class):
    tile_dev, date_dev, extent, _, channels = stacks.shape
    frames = stacks.reshape(tile_dev * date_dev, extent, extent, channels)
    pre_act = spatial_forward(frames, w_spatial)
    activation, h_slope = silu_pair(pre_act)
    valid_float = valid.astype(jnp.float32)
    pooled = block_mean(activation).reshape(tile_dev, date_dev, -1, channels)
    blocks = pooled.shape[2]
    pooled_b = (pooled * valid_float[:, :, None, None]).astype(jnp.bfloat16)
    date_count = lax.axis_size("date")
    date_total = date_count * date_dev
    share = blocks // date_count
    share_start = lax.axis_index("date") * share
    date_start = lax.axis_index("date") * date_dev
    every_date = date_gather(pooled_b)
    extended = jnp.pad(every_date, ((0, 0), (2, 2), (0, 0), (0, 0)))
    response, response_slope = silu_pair(temporal_forward(extended, w_temporal, date_total))
    summary = jnp.sum(response, axis=1) / date_total
    summary_b = summary.astype(jnp.bfloat16)
    class_slope, back_sum = classify(summary_b, labels, w_class)
    own_summary = lax.dynamic_slice_in_dim(summary_b, share_start, share, 1)
    own_slope = lax.dynamic_slice_in_dim(class_slope, share_start, share, 1)
    grad_class = jnp.einsum(
        "tbc,tbk->ck", own_summary, own_slope, preferred_element_type=jnp.float32
    )
    scaled = back_sum / date_total
    back_q = (scaled[:, None] * response_slope).astype(jnp.bfloat16)
    own_q = lax.dynamic_slice_in_dim(back_q, date_start, date_dev, 1)
    back_ext = jnp.pad(back_q, ((0, 0), (2, 2), (0, 0), (0, 0)))
    taps = w_temporal.shape[0]
    grad_temporal = jnp.stack(
        [
            jnp.einsum(
                "tdbc,tdbe->ce",
                lax.dynamic_slice_in_dim(extended, date_start + offset, date_dev, 1),
                own_q,
                preferred_element_type=jnp.float32,
            )
            for offset in range(taps)
        ]
    )
    back_pool = jnp.zeros(pooled.shape, jnp.float32)
    for offset in range(taps):
        back_pool = back_pool + jnp.einsum(
            "tdbe,ce->tdbc",
            lax.dynamic_slice_in_dim(back_ext, date_start + 4 - offset, date_dev, 1),
            w_temporal[offset],
            preferred_element_type=jnp.float32,
        )
    back_block = (back_pool * valid_float[:, :, None, None] / (POOL * POOL)).reshape(
        tile_dev * date_dev, blocks, channels
    )
    back_h = (block_spread(back_block, extent) * h_slope).astype(jnp.bfloat16)
    windows = spatial_windows(frames)
    grad_spatial = jnp.stack(
        [
            jnp.einsum("fyxc,fyxe->ce", window, back_h, preferred_element_type=jnp.float32)
            for window in windows
        ]
    ).reshape(3, 3, channels, channels)
    total_spatial, total_temporal, total_class = all_sum(
        (grad_spatial, grad_temporal, grad_class)
    )
    return (normalize(total_spatial), normalize(total_temporal), normalize(total_class))


def solution(mesh):
    in_specs = (
        P("tile", "date", None, None, None),
        P("tile", "date"),
        P("tile", None),
        P(),
        P(),
        P(),
    )
    out_specs = (P(), P(), P())
    return jax.shard_map(shards, mesh=mesh, in_specs=in_specs, out_specs=out_specs, check_vma=False)
```

```python
import jax
import jax.numpy as jnp
from jax import lax
from jax.sharding import PartitionSpec as P

POOL = 8


EPSILON = 1e-06


def padded_2(block, sides, width):
    for axis, dim in sides:
        count = lax.axis_size(axis)
        forward = [(i, i + 1) for i in range(count - 1)]
        backward = [(target, source) for source, target in forward]
        low = lax.ppermute(
            lax.slice_in_dim(block, block.shape[dim] - width, None, axis=dim), axis, forward
        )
        high = lax.ppermute(lax.slice_in_dim(block, 0, width, axis=dim), axis, backward)
        block = jnp.concatenate([low, block, high], axis=dim)
    return block


def silu_pair(value):
    sigma = jax.nn.sigmoid(value)
    return (value * sigma, sigma * (1.0 + value * (1.0 - sigma)))


def spatial_windows(frames):
    extent = frames.shape[1]
    padded = jnp.pad(frames, ((0, 0), (1, 1), (1, 1), (0, 0)))
    return [
        padded[:, row_shift : row_shift + extent, col_shift : col_shift + extent, :]
        for row_shift in range(3)
        for col_shift in range(3)
    ]


def spatial_forward(frames, w_spatial):
    return lax.conv_general_dilated(
        frames,
        w_spatial,
        (1, 1),
        ((1, 1), (1, 1)),
        dimension_numbers=("NHWC", "HWIO", "NHWC"),
        preferred_element_type=jnp.float32,
    )


def date_sum(value):
    count = lax.axis_size("date")
    mask = 1
    while mask < count:
        value = value + lax.ppermute(value, "date", [(i, i ^ mask) for i in range(count)])
        mask *= 2
    return value


def block_mean(activation):
    frames, extent, _, channels = activation.shape
    per_side = extent // POOL
    shaped = activation.reshape(frames, per_side, POOL, per_side, POOL, channels)
    return jnp.mean(shaped, axis=(2, 4)).reshape(frames, per_side * per_side, channels)


def block_spread(block_values, extent):
    frames, _, channels = block_values.shape
    per_side = extent // POOL
    spread = jnp.broadcast_to(
        block_values.reshape(frames, per_side, 1, per_side, 1, channels),
        (frames, per_side, POOL, per_side, POOL, channels),
    )
    return spread.reshape(frames, extent, extent, channels)


def swap_blocks(values):
    frames, blocks, channels = values.shape
    per_side = int(round(blocks**0.5))
    shaped = values.reshape(frames, per_side, per_side, channels)
    return jnp.swapaxes(shaped, 1, 2).reshape(frames, blocks, channels)


def temporal_forward(extended, w_temporal, count):
    running = jnp.zeros(
        (extended.shape[0], count, extended.shape[2], extended.shape[3]), jnp.float32
    )
    for offset in range(w_temporal.shape[0]):
        running = running + jnp.einsum(
            "tdbc,ce->tdbe",
            extended[:, offset : offset + count],
            w_temporal[offset],
            preferred_element_type=jnp.float32,
        )
    return running


def classify(summary_b, label_rows, w_class):
    logits = jnp.einsum("tbc,ck->tbk", summary_b, w_class, preferred_element_type=jnp.float32)
    exponent = jnp.exp(logits)
    probability = exponent / jnp.sum(exponent, axis=-1, keepdims=True)
    onehot = (
        label_rows[:, :, None] == jnp.arange(w_class.shape[1], dtype=jnp.int32)[None, None, :]
    ).astype(jnp.float32)
    class_slope = (probability - onehot).astype(jnp.bfloat16)
    back_sum = jnp.einsum("tbk,ck->tbc", class_slope, w_class, preferred_element_type=jnp.float32)
    return (class_slope, back_sum)


def normalize(gradient):
    return gradient / jnp.sqrt(jnp.mean(gradient * gradient) + EPSILON)


def exchange_groups():
    tile_bits = lax.axis_size("tile").bit_length() - 1
    date_bits = lax.axis_size("date").bit_length() - 1
    assert 1 << tile_bits == lax.axis_size("tile") and 1 << date_bits == lax.axis_size("date")
    if tile_bits == 6 and date_bits == 2:
        return [[2], [5, 0, 1], [3, 4], [6, 7]]
    return [[bit] for bit in range(tile_bits + date_bits)]


def group_code(index, bits):
    code = 0
    for place, bit in enumerate(bits):
        code = code + ((index >> bit) & 1) * (1 << place)
    return code


def group_mask(code, bits):
    return sum(1 << bit for place, bit in enumerate(bits) if (code >> place) & 1)


def all_sum(parts):
    lanes = 128
    axes = ("tile", "date")
    total = lax.axis_size("tile") * lax.axis_size("date")
    index = lax.axis_index("tile") * lax.axis_size("date") + lax.axis_index("date")
    flat = jnp.concatenate([part.reshape(-1) for part in parts])
    groups = exchange_groups()
    unit = 8 * total
    rows = -(-flat.shape[0] // (lanes * unit)) * unit
    buf = jnp.pad(flat, (0, rows * lanes - flat.shape[0])).reshape(rows, lanes)
    for bits in groups:
        size = buf.shape[0] >> len(bits)
        own = group_code(index, bits)
        acc = lax.dynamic_slice_in_dim(buf, own * size, size)
        for code in range(1, 1 << len(bits)):
            mask = group_mask(code, bits)
            send = lax.dynamic_slice_in_dim(buf, (own ^ code) * size, size)
            acc = acc + lax.ppermute(send, axes, [(i, i ^ mask) for i in range(total)])
        buf = acc
    for bits in reversed(groups):
        size = buf.shape[0]
        own = group_code(index, bits)
        out = jnp.zeros((size << len(bits), lanes), buf.dtype)
        out = lax.dynamic_update_slice_in_dim(out, buf, own * size, 0)
        for code in range(1, 1 << len(bits)):
            mask = group_mask(code, bits)
            got = lax.ppermute(buf, axes, [(i, i ^ mask) for i in range(total)])
            out = lax.dynamic_update_slice_in_dim(out, got, (own ^ code) * size, 0)
        buf = out
    flat = buf.reshape(-1)
    out, start = [], 0
    for part in parts:
        out.append(flat[start : start + part.size].reshape(part.shape))
        start += part.size
    return out


def date_gather(block):
    count = lax.axis_size("date")
    own = lax.axis_index("date")
    depth = block.shape[1]
    shape = (block.shape[0], depth * count) + block.shape[2:]
    out = lax.dynamic_update_slice_in_dim(jnp.zeros(shape, block.dtype), block, own * depth, 1)
    for mask in range(1, count):
        got = lax.ppermute(block, "date", [(i, i ^ mask) for i in range(count)])
        out = lax.dynamic_update_slice_in_dim(out, got, (own ^ mask) * depth, 1)
    return out


def shards(stacks, valid, labels, w_spatial, w_temporal, w_class):
    tile_dev, date_dev, extent, _, channels = stacks.shape
    frames = jnp.swapaxes(stacks.reshape(tile_dev * date_dev, extent, extent, channels), 1, 2)
    pre_act = spatial_forward(frames, jnp.swapaxes(w_spatial, 0, 1))
    activation, h_slope = silu_pair(pre_act)
    valid_float = valid.astype(jnp.float32)
    pooled = swap_blocks(block_mean(activation)).reshape(tile_dev, date_dev, -1, channels)
    blocks = pooled.shape[2]
    pooled_b = (pooled * valid_float[:, :, None, None]).astype(jnp.bfloat16)
    date_count = lax.axis_size("date")
    date_total = date_count * date_dev
    share = blocks // date_count
    share_start = lax.axis_index("date") * share
    date_start = lax.axis_index("date") * date_dev
    every_date = date_gather(pooled_b)
    extended = jnp.pad(every_date, ((0, 0), (2, 2), (0, 0), (0, 0)))
    response, response_slope = silu_pair(temporal_forward(extended, w_temporal, date_total))
    summary = jnp.sum(response, axis=1) / date_total
    summary_b = summary.astype(jnp.bfloat16)
    class_slope, back_sum = classify(summary_b, labels, w_class)
    own_summary = lax.dynamic_slice_in_dim(summary_b, share_start, share, 1)
    own_slope = lax.dynamic_slice_in_dim(class_slope, share_start, share, 1)
    grad_class = jnp.einsum(
        "tbc,tbk->ck", own_summary, own_slope, preferred_element_type=jnp.float32
    )
    scaled = back_sum / date_total
    back_q = (scaled[:, None] * response_slope).astype(jnp.bfloat16)
    own_q = lax.dynamic_slice_in_dim(back_q, date_start, date_dev, 1)
    back_ext = jnp.pad(back_q, ((0, 0), (2, 2), (0, 0), (0, 0)))
    taps = w_temporal.shape[0]
    grad_temporal = jnp.stack(
        [
            jnp.einsum(
                "tdbc,tdbe->ce",
                lax.dynamic_slice_in_dim(extended, date_start + offset, date_dev, 1),
                own_q,
                preferred_element_type=jnp.float32,
            )
            for offset in range(taps)
        ]
    )
    back_pool = jnp.zeros(pooled.shape, jnp.float32)
    for offset in range(taps):
        back_pool = back_pool + jnp.einsum(
            "tdbe,ce->tdbc",
            lax.dynamic_slice_in_dim(back_ext, date_start + 4 - offset, date_dev, 1),
            w_temporal[offset],
            preferred_element_type=jnp.float32,
        )
    back_block = (back_pool * valid_float[:, :, None, None] / (POOL * POOL)).reshape(
        tile_dev * date_dev, blocks, channels
    )
    back_h = (block_spread(swap_blocks(back_block), extent) * h_slope).astype(jnp.bfloat16)
    windows = spatial_windows(frames)
    grad_spatial = jnp.stack(
        [
            jnp.einsum("fyxc,fyxe->ce", window, back_h, preferred_element_type=jnp.float32)
            for window in windows
        ]
    ).reshape(3, 3, channels, channels)
    grad_spatial = jnp.swapaxes(grad_spatial, 0, 1)
    total_spatial, total_temporal, total_class = all_sum(
        (grad_spatial, grad_temporal, grad_class)
    )
    return (normalize(total_spatial), normalize(total_temporal), normalize(total_class))


def solution(mesh):
    in_specs = (
        P("tile", "date", None, None, None),
        P("tile", "date"),
        P("tile", None),
        P(),
        P(),
        P(),
    )
    out_specs = (P(), P(), P())
    return jax.shard_map(shards, mesh=mesh, in_specs=in_specs, out_specs=out_specs, check_vma=False)
```

```python
import jax
import jax.numpy as jnp
from jax import lax
from jax.sharding import PartitionSpec as P

POOL = 8


EPSILON = 1e-06


def padded_2(block, sides, width):
    for axis, dim in sides:
        count = lax.axis_size(axis)
        forward = [(i, i + 1) for i in range(count - 1)]
        backward = [(target, source) for source, target in forward]
        low = lax.ppermute(
            lax.slice_in_dim(block, block.shape[dim] - width, None, axis=dim), axis, forward
        )
        high = lax.ppermute(lax.slice_in_dim(block, 0, width, axis=dim), axis, backward)
        block = jnp.concatenate([low, block, high], axis=dim)
    return block


def silu_pair(value):
    sigma = jax.nn.sigmoid(value)
    return (value * sigma, sigma * (1.0 + value * (1.0 - sigma)))


def spatial_windows(frames):
    extent = frames.shape[1]
    padded = jnp.pad(frames, ((0, 0), (1, 1), (1, 1), (0, 0)))
    return [
        padded[:, row_shift : row_shift + extent, col_shift : col_shift + extent, :]
        for row_shift in range(3)
        for col_shift in range(3)
    ]


def spatial_forward(frames, w_spatial):
    return lax.conv_general_dilated(
        frames,
        w_spatial,
        (1, 1),
        ((1, 1), (1, 1)),
        dimension_numbers=("NHWC", "HWIO", "NHWC"),
        preferred_element_type=jnp.float32,
    )


def date_sum(value):
    count = lax.axis_size("date")
    mask = 1
    while mask < count:
        value = value + lax.ppermute(value, "date", [(i, i ^ mask) for i in range(count)])
        mask *= 2
    return value


def block_mean(activation):
    frames, extent, _, channels = activation.shape
    per_side = extent // POOL
    shaped = activation.reshape(frames, per_side, POOL, per_side, POOL, channels)
    return jnp.mean(shaped, axis=(2, 4)).reshape(frames, per_side * per_side, channels)


def block_spread(block_values, extent):
    frames, _, channels = block_values.shape
    per_side = extent // POOL
    spread = jnp.broadcast_to(
        block_values.reshape(frames, per_side, 1, per_side, 1, channels),
        (frames, per_side, POOL, per_side, POOL, channels),
    )
    return spread.reshape(frames, extent, extent, channels)


def swap_blocks(values):
    frames, blocks, channels = values.shape
    per_side = int(round(blocks**0.5))
    shaped = values.reshape(frames, per_side, per_side, channels)
    return jnp.swapaxes(shaped, 1, 2).reshape(frames, blocks, channels)


def temporal_forward(extended, w_temporal, count):
    running = jnp.zeros(
        (extended.shape[0], count, extended.shape[2], extended.shape[3]), jnp.float32
    )
    for offset in range(w_temporal.shape[0]):
        running = running + jnp.einsum(
            "tdbc,ce->tdbe",
            extended[:, offset : offset + count],
            w_temporal[offset],
            preferred_element_type=jnp.float32,
        )
    return running


def classify(summary_b, label_rows, w_class):
    logits = jnp.einsum("tbc,ck->tbk", summary_b, w_class, preferred_element_type=jnp.float32)
    exponent = jnp.exp(logits)
    probability = exponent / jnp.sum(exponent, axis=-1, keepdims=True)
    onehot = (
        label_rows[:, :, None] == jnp.arange(w_class.shape[1], dtype=jnp.int32)[None, None, :]
    ).astype(jnp.float32)
    class_slope = (probability - onehot).astype(jnp.bfloat16)
    back_sum = jnp.einsum("tbk,ck->tbc", class_slope, w_class, preferred_element_type=jnp.float32)
    return (class_slope, back_sum)


def normalize(gradient):
    return gradient / jnp.sqrt(jnp.mean(gradient * gradient) + EPSILON)


def exchange_groups():
    tile_bits = lax.axis_size("tile").bit_length() - 1
    date_bits = lax.axis_size("date").bit_length() - 1
    assert 1 << tile_bits == lax.axis_size("tile") and 1 << date_bits == lax.axis_size("date")
    if tile_bits == 6 and date_bits == 2:
        return [[2], [5, 0, 1], [3, 4], [6, 7]]
    return [[bit] for bit in range(tile_bits + date_bits)]


def group_code(index, bits):
    code = 0
    for place, bit in enumerate(bits):
        code = code + ((index >> bit) & 1) * (1 << place)
    return code


def group_mask(code, bits):
    return sum(1 << bit for place, bit in enumerate(bits) if (code >> place) & 1)


def all_sum(parts):
    lanes = 128
    axes = ("tile", "date")
    total = lax.axis_size("tile") * lax.axis_size("date")
    index = lax.axis_index("tile") * lax.axis_size("date") + lax.axis_index("date")
    flat = jnp.concatenate([part.reshape(-1) for part in parts])
    groups = exchange_groups()
    unit = 8 * total
    rows = -(-flat.shape[0] // (lanes * unit)) * unit
    buf = jnp.pad(flat, (0, rows * lanes - flat.shape[0])).reshape(rows, lanes)
    for bits in groups:
        size = buf.shape[0] >> len(bits)
        own = group_code(index, bits)
        acc = lax.dynamic_slice_in_dim(buf, own * size, size)
        for code in range(1, 1 << len(bits)):
            mask = group_mask(code, bits)
            send = lax.dynamic_slice_in_dim(buf, (own ^ code) * size, size)
            acc = acc + lax.ppermute(send, axes, [(i, i ^ mask) for i in range(total)])
        buf = acc
    for bits in reversed(groups):
        size = buf.shape[0]
        own = group_code(index, bits)
        out = jnp.zeros((size << len(bits), lanes), buf.dtype)
        out = lax.dynamic_update_slice_in_dim(out, buf, own * size, 0)
        for code in range(1, 1 << len(bits)):
            mask = group_mask(code, bits)
            got = lax.ppermute(buf, axes, [(i, i ^ mask) for i in range(total)])
            out = lax.dynamic_update_slice_in_dim(out, got, (own ^ code) * size, 0)
        buf = out
    row_squares = jnp.sum(buf * buf, axis=1)
    row = lax.broadcasted_iota(jnp.int32, (buf.shape[0], 1), 0)
    denom = jnp.ones((buf.shape[0], 1), jnp.float32)
    start = 0
    for part in parts:
        first, last = start // lanes, (start + part.size) // lanes
        mean = jnp.sum(row_squares[first:last]) / part.size
        inside = (row >= first) & (row < last)
        denom = jnp.where(inside, jnp.sqrt(mean + EPSILON), denom)
        start += part.size
    flat = (buf / denom).reshape(-1)
    out, start = [], 0
    for part in parts:
        out.append(flat[start : start + part.size].reshape(part.shape))
        start += part.size
    return out


def date_gather(block):
    count = lax.axis_size("date")
    own = lax.axis_index("date")
    depth = block.shape[1]
    shape = (block.shape[0], depth * count) + block.shape[2:]
    out = lax.dynamic_update_slice_in_dim(jnp.zeros(shape, block.dtype), block, own * depth, 1)
    for mask in range(1, count):
        got = lax.ppermute(block, "date", [(i, i ^ mask) for i in range(count)])
        out = lax.dynamic_update_slice_in_dim(out, got, (own ^ mask) * depth, 1)
    return out


def shards(stacks, valid, labels, w_spatial, w_temporal, w_class):
    tile_dev, date_dev, extent, _, channels = stacks.shape
    frames = jnp.swapaxes(stacks.reshape(tile_dev * date_dev, extent, extent, channels), 1, 2)
    pre_act = spatial_forward(frames, jnp.swapaxes(w_spatial, 0, 1))
    activation, h_slope = silu_pair(pre_act)
    valid_float = valid.astype(jnp.float32)
    pooled = swap_blocks(block_mean(activation)).reshape(tile_dev, date_dev, -1, channels)
    blocks = pooled.shape[2]
    pooled_b = (pooled * valid_float[:, :, None, None]).astype(jnp.bfloat16)
    date_count = lax.axis_size("date")
    date_total = date_count * date_dev
    share = blocks // date_count
    share_start = lax.axis_index("date") * share
    date_start = lax.axis_index("date") * date_dev
    every_date = date_gather(pooled_b)
    extended = jnp.pad(every_date, ((0, 0), (2, 2), (0, 0), (0, 0)))
    response, response_slope = silu_pair(temporal_forward(extended, w_temporal, date_total))
    summary = jnp.sum(response, axis=1) / date_total
    summary_b = summary.astype(jnp.bfloat16)
    class_slope, back_sum = classify(summary_b, labels, w_class)
    own_summary = lax.dynamic_slice_in_dim(summary_b, share_start, share, 1)
    own_slope = lax.dynamic_slice_in_dim(class_slope, share_start, share, 1)
    grad_class = jnp.einsum(
        "tbc,tbk->ck", own_summary, own_slope, preferred_element_type=jnp.float32
    )
    scaled = back_sum / date_total
    back_q = (scaled[:, None] * response_slope).astype(jnp.bfloat16)
    own_q = lax.dynamic_slice_in_dim(back_q, date_start, date_dev, 1)
    back_ext = jnp.pad(back_q, ((0, 0), (2, 2), (0, 0), (0, 0)))
    taps = w_temporal.shape[0]
    grad_temporal = jnp.stack(
        [
            jnp.einsum(
                "tdbc,tdbe->ce",
                lax.dynamic_slice_in_dim(extended, date_start + offset, date_dev, 1),
                own_q,
                preferred_element_type=jnp.float32,
            )
            for offset in range(taps)
        ]
    )
    back_pool = jnp.zeros(pooled.shape, jnp.float32)
    for offset in range(taps):
        back_pool = back_pool + jnp.einsum(
            "tdbe,ce->tdbc",
            lax.dynamic_slice_in_dim(back_ext, date_start + 4 - offset, date_dev, 1),
            w_temporal[offset],
            preferred_element_type=jnp.float32,
        )
    back_block = (back_pool * valid_float[:, :, None, None] / (POOL * POOL)).reshape(
        tile_dev * date_dev, blocks, channels
    )
    back_h = (block_spread(swap_blocks(back_block), extent) * h_slope).astype(jnp.bfloat16)
    windows = spatial_windows(frames)
    grad_spatial = jnp.stack(
        [
            jnp.einsum("fyxc,fyxe->ce", window, back_h, preferred_element_type=jnp.float32)
            for window in windows
        ]
    ).reshape(3, 3, channels, channels)
    grad_spatial = jnp.swapaxes(grad_spatial, 0, 1)
    total_spatial, total_temporal, total_class = all_sum(
        (grad_spatial, grad_temporal, grad_class)
    )
    return (total_spatial, total_temporal, total_class)


def solution(mesh):
    in_specs = (
        P("tile", "date", None, None, None),
        P("tile", "date"),
        P("tile", None),
        P(),
        P(),
        P(),
    )
    out_specs = (P(), P(), P())
    return jax.shard_map(shards, mesh=mesh, in_specs=in_specs, out_specs=out_specs, check_vma=False)
```

```python
import jax
import jax.numpy as jnp
from jax import lax
from jax.sharding import PartitionSpec as P

POOL = 8


EPSILON = 1e-06


def padded_2(block, sides, width):
    for axis, dim in sides:
        count = lax.axis_size(axis)
        forward = [(i, i + 1) for i in range(count - 1)]
        backward = [(target, source) for source, target in forward]
        low = lax.ppermute(
            lax.slice_in_dim(block, block.shape[dim] - width, None, axis=dim), axis, forward
        )
        high = lax.ppermute(lax.slice_in_dim(block, 0, width, axis=dim), axis, backward)
        block = jnp.concatenate([low, block, high], axis=dim)
    return block


def silu_pair(value):
    sigma = jax.nn.sigmoid(value)
    return (value * sigma, sigma * (1.0 + value * (1.0 - sigma)))


def spatial_windows(frames):
    extent = frames.shape[1]
    padded = jnp.pad(frames, ((0, 0), (1, 1), (1, 1), (0, 0)))
    return [
        padded[:, row_shift : row_shift + extent, col_shift : col_shift + extent, :]
        for row_shift in range(3)
        for col_shift in range(3)
    ]


def spatial_forward(frames, w_spatial):
    return lax.conv_general_dilated(
        frames,
        w_spatial,
        (1, 1),
        ((1, 1), (1, 1)),
        dimension_numbers=("NHWC", "HWIO", "NHWC"),
        preferred_element_type=jnp.float32,
    )


def date_sum(value):
    count = lax.axis_size("date")
    mask = 1
    while mask < count:
        value = value + lax.ppermute(value, "date", [(i, i ^ mask) for i in range(count)])
        mask *= 2
    return value


def block_mean(activation):
    frames, extent, _, channels = activation.shape
    per_side = extent // POOL
    shaped = activation.reshape(frames, per_side, POOL, per_side, POOL, channels)
    partial = lax.optimization_barrier(jnp.sum(shaped, axis=4))
    total = jnp.sum(partial, axis=2) / (POOL * POOL)
    return total.reshape(frames, per_side * per_side, channels)


def block_spread(block_values, extent):
    frames, _, channels = block_values.shape
    per_side = extent // POOL
    spread = jnp.broadcast_to(
        block_values.reshape(frames, per_side, 1, per_side, 1, channels),
        (frames, per_side, POOL, per_side, POOL, channels),
    )
    return spread.reshape(frames, extent, extent, channels)


def swap_blocks(values):
    frames, blocks, channels = values.shape
    per_side = int(round(blocks**0.5))
    shaped = values.reshape(frames, per_side, per_side, channels)
    return jnp.swapaxes(shaped, 1, 2).reshape(frames, blocks, channels)


def temporal_forward(extended, w_temporal, count):
    running = jnp.zeros(
        (extended.shape[0], count, extended.shape[2], extended.shape[3]), jnp.float32
    )
    for offset in range(w_temporal.shape[0]):
        running = running + jnp.einsum(
            "tdbc,ce->tdbe",
            extended[:, offset : offset + count],
            w_temporal[offset],
            preferred_element_type=jnp.float32,
        )
    return running


def classify(summary_b, label_rows, w_class):
    logits = jnp.einsum("tbc,ck->tbk", summary_b, w_class, preferred_element_type=jnp.float32)
    exponent = jnp.exp(logits)
    probability = exponent / jnp.sum(exponent, axis=-1, keepdims=True)
    onehot = (
        label_rows[:, :, None] == jnp.arange(w_class.shape[1], dtype=jnp.int32)[None, None, :]
    ).astype(jnp.float32)
    class_slope = (probability - onehot).astype(jnp.bfloat16)
    back_sum = jnp.einsum("tbk,ck->tbc", class_slope, w_class, preferred_element_type=jnp.float32)
    return (class_slope, back_sum)


def normalize(gradient):
    return gradient / jnp.sqrt(jnp.mean(gradient * gradient) + EPSILON)


def exchange_groups():
    tile_bits = lax.axis_size("tile").bit_length() - 1
    date_bits = lax.axis_size("date").bit_length() - 1
    assert 1 << tile_bits == lax.axis_size("tile") and 1 << date_bits == lax.axis_size("date")
    if tile_bits == 6 and date_bits == 2:
        return [[2], [5, 0, 1], [3, 4], [6, 7]]
    return [[bit] for bit in range(tile_bits + date_bits)]


def group_code(index, bits):
    code = 0
    for place, bit in enumerate(bits):
        code = code + ((index >> bit) & 1) * (1 << place)
    return code


def group_mask(code, bits):
    return sum(1 << bit for place, bit in enumerate(bits) if (code >> place) & 1)


def all_sum(parts):
    lanes = 128
    axes = ("tile", "date")
    total = lax.axis_size("tile") * lax.axis_size("date")
    index = lax.axis_index("tile") * lax.axis_size("date") + lax.axis_index("date")
    flat = jnp.concatenate([part.reshape(-1) for part in parts])
    groups = exchange_groups()
    unit = 8 * total
    rows = -(-flat.shape[0] // (lanes * unit)) * unit
    buf = jnp.pad(flat, (0, rows * lanes - flat.shape[0])).reshape(rows, lanes)
    for bits in groups:
        size = buf.shape[0] >> len(bits)
        own = group_code(index, bits)
        acc = lax.dynamic_slice_in_dim(buf, own * size, size)
        for code in range(1, 1 << len(bits)):
            mask = group_mask(code, bits)
            send = lax.dynamic_slice_in_dim(buf, (own ^ code) * size, size)
            acc = acc + lax.ppermute(send, axes, [(i, i ^ mask) for i in range(total)])
        buf = acc
    for bits in reversed(groups):
        size = buf.shape[0]
        own = group_code(index, bits)
        out = jnp.zeros((size << len(bits), lanes), buf.dtype)
        out = lax.dynamic_update_slice_in_dim(out, buf, own * size, 0)
        for code in range(1, 1 << len(bits)):
            mask = group_mask(code, bits)
            got = lax.ppermute(buf, axes, [(i, i ^ mask) for i in range(total)])
            out = lax.dynamic_update_slice_in_dim(out, got, (own ^ code) * size, 0)
        buf = out
    flat = buf.reshape(-1)
    out, start = [], 0
    for part in parts:
        out.append(flat[start : start + part.size].reshape(part.shape))
        start += part.size
    return out


def date_gather(block):
    count = lax.axis_size("date")
    own = lax.axis_index("date")
    depth = block.shape[1]
    shape = (block.shape[0], depth * count) + block.shape[2:]
    out = lax.dynamic_update_slice_in_dim(jnp.zeros(shape, block.dtype), block, own * depth, 1)
    for mask in range(1, count):
        got = lax.ppermute(block, "date", [(i, i ^ mask) for i in range(count)])
        out = lax.dynamic_update_slice_in_dim(out, got, (own ^ mask) * depth, 1)
    return out


def shards(stacks, valid, labels, w_spatial, w_temporal, w_class):
    tile_dev, date_dev, extent, _, channels = stacks.shape
    frames = jnp.swapaxes(stacks.reshape(tile_dev * date_dev, extent, extent, channels), 1, 2)
    pre_act = spatial_forward(frames, jnp.swapaxes(w_spatial, 0, 1))
    activation, h_slope = silu_pair(pre_act)
    valid_float = valid.astype(jnp.float32)
    pooled = swap_blocks(block_mean(activation)).reshape(tile_dev, date_dev, -1, channels)
    blocks = pooled.shape[2]
    pooled_b = (pooled * valid_float[:, :, None, None]).astype(jnp.bfloat16)
    date_count = lax.axis_size("date")
    date_total = date_count * date_dev
    share = blocks // date_count
    share_start = lax.axis_index("date") * share
    date_start = lax.axis_index("date") * date_dev
    every_date = date_gather(pooled_b)
    extended = jnp.pad(every_date, ((0, 0), (2, 2), (0, 0), (0, 0)))
    response, response_slope = silu_pair(temporal_forward(extended, w_temporal, date_total))
    summary = jnp.sum(response, axis=1) / date_total
    summary_b = summary.astype(jnp.bfloat16)
    class_slope, back_sum = classify(summary_b, labels, w_class)
    own_summary = lax.dynamic_slice_in_dim(summary_b, share_start, share, 1)
    own_slope = lax.dynamic_slice_in_dim(class_slope, share_start, share, 1)
    grad_class = jnp.einsum(
        "tbc,tbk->ck", own_summary, own_slope, preferred_element_type=jnp.float32
    )
    scaled = back_sum / date_total
    back_q = (scaled[:, None] * response_slope).astype(jnp.bfloat16)
    own_q = lax.dynamic_slice_in_dim(back_q, date_start, date_dev, 1)
    back_ext = jnp.pad(back_q, ((0, 0), (2, 2), (0, 0), (0, 0)))
    taps = w_temporal.shape[0]
    grad_temporal = jnp.stack(
        [
            jnp.einsum(
                "tdbc,tdbe->ce",
                lax.dynamic_slice_in_dim(extended, date_start + offset, date_dev, 1),
                own_q,
                preferred_element_type=jnp.float32,
            )
            for offset in range(taps)
        ]
    )
    back_pool = jnp.zeros(pooled.shape, jnp.float32)
    for offset in range(taps):
        back_pool = back_pool + jnp.einsum(
            "tdbe,ce->tdbc",
            lax.dynamic_slice_in_dim(back_ext, date_start + 4 - offset, date_dev, 1),
            w_temporal[offset],
            preferred_element_type=jnp.float32,
        )
    back_block = (back_pool * valid_float[:, :, None, None] / (POOL * POOL)).reshape(
        tile_dev * date_dev, blocks, channels
    )
    back_h = (block_spread(swap_blocks(back_block), extent) * h_slope).astype(jnp.bfloat16)
    windows = spatial_windows(frames)
    grad_spatial = jnp.stack(
        [
            jnp.einsum("fyxc,fyxe->ce", window, back_h, preferred_element_type=jnp.float32)
            for window in windows
        ]
    ).reshape(3, 3, channels, channels)
    grad_spatial = jnp.swapaxes(grad_spatial, 0, 1)
    total_spatial, total_temporal, total_class = all_sum(
        (grad_spatial, grad_temporal, grad_class)
    )
    return (normalize(total_spatial), normalize(total_temporal), normalize(total_class))


def solution(mesh):
    in_specs = (
        P("tile", "date", None, None, None),
        P("tile", "date"),
        P("tile", None),
        P(),
        P(),
        P(),
    )
    out_specs = (P(), P(), P())
    return jax.shard_map(shards, mesh=mesh, in_specs=in_specs, out_specs=out_specs, check_vma=False)
```
